256 devices in a mesh: scan: 8 (over x, core), mode: 32 (over y, z).
Axes of the slice: x: 4, y: 4, z: 8, core: 2. Of those that a mesh axis runs over, the one named last changes fastest.
Arguments:
- object_field: float32 [2, 2048, 1024], P(None, 'scan'), may hold values from -5 to 5
- probe_modes: float32 [2, 32, 128, 128], P(None, 'mode'), may hold values from -9 to 9
- scan_offsets: int32 [2, 256], P(None, 'scan'), may hold values from 0 to 896, as said below
- measured: float32 [256, 128, 128], P('scan'), may hold values from 0.05 to 3
Outputs:
- object_new: float32 [2, 2048, 1024], P(None, ('scan', 'mode'))
- probe_new: float32 [2, 32, 128, 128], P(None, 'mode')
The draws below stay inside these ranges and needn't reach their ends.
Inputs may be any that keep to these rules, and one draw needn't show every extreme that they name: scan_offsets[0, j] lies in 0 to 128 and scan_offsets[1, j] in 0 to 896; position j belongs to tile j // 32.
All inputs are finite; a program needn't handle non-finite values.
Results may differ from the reference program's by a relative error of at most 0.0027.
Values sent between devices are 32-bit elements; how exact they have to be, the bound alone decides.
No kernel may reach another device: no remote copies, remote signals or barrier semaphores. Data moves between devices by JAX's collectives and lax.ppermute only.
A program may use at most 128 MiB of HBM per device.

```python
import math
import jax
import jax.numpy as jnp
from jax import lax

M = 128
K = 32
TILE_R = 256
OBJ_C = 1024
NS_ITERS = 8
J_SC = 32
J = 256
OBJ_R = 2048


def draw_scan_offsets(key, part):
    key_row, key_col = jax.random.split(jax.random.fold_in(key, 7))
    row_starts = jax.random.randint(key_row, (J,), 0, TILE_R - M + 1, dtype=jnp.int32)
    col_starts = jax.random.randint(key_col, (J,), 0, OBJ_C - M + 1, dtype=jnp.int32)
    row_starts = row_starts.at[0].set(TILE_R - M).at[1].set(0)
    col_starts = col_starts.at[0].set(OBJ_C - M).at[1].set(0)
    return jnp.stack([row_starts, col_starts])


def draw_probe_modes(key, part):
    key_own, key_common, key_power = jax.random.split(jax.random.fold_in(key, 13), 3)
    own_part = jnp.clip(jax.random.normal(key_own, (2, K, M, M), jnp.float32), -5.0, 5.0)
    common_part = jnp.clip(jax.random.normal(key_common, (2, 1, M, M), jnp.float32), -5.0, 5.0)
    mode_power = jnp.exp(jax.random.uniform(key_power, (1, K, 1, 1), jnp.float32, math.log(0.15), 0.0))
    return (mode_power * (0.7 * common_part + own_part) / math.sqrt(K)).astype(jnp.float32)


def level_of(stream_key, extent, cuts, low, top_value):
    loudness, own = 1.0, jax.random.fold_in(stream_key, 6)
    for dim, parts in cuts:
        heights = jnp.exp(jax.random.uniform(jax.random.fold_in(own, dim), (parts,), jnp.float32, low / len(cuts), top_value / len(cuts)))
        loudness = loudness * jnp.repeat(heights, extent[dim] // parts).reshape([-1 if axis == dim else 1 for axis in range(len(extent))])
    return loudness


def centred(stream_key, dims, scale, reach, cuts=(), held_as=jnp.bfloat16):
    drawn = scale * jax.random.normal(stream_key, dims, jnp.float32)
    if cuts:
        drawn = drawn * level_of(stream_key, dims, cuts, -0.22, 0.18)
    return jnp.clip(drawn, -reach, reach).astype(held_as)


def setup_inputs(seed: int = 0) -> dict:
    keys = jax.random.split(jax.random.key(seed), 5)
    return {
        "object_field": centred(keys[0], (2, OBJ_R, OBJ_C), 0.8, 5.0, ((1, 8),), jnp.float32),
        "probe_modes": draw_probe_modes(jax.random.fold_in(keys[4], 71), 0),
        "scan_offsets": draw_scan_offsets(jax.random.fold_in(keys[4], 71), 0),
        "measured": jnp.clip(jnp.exp(math.log(3.0) - 4.0943445 * jax.random.uniform(keys[3], (J, M, M), jnp.float32) ** level_of(keys[3], (J, M, M), ((0, 8),), -0.2, 0.2)), 0.05, 3.0),
    }


FLOOR_INTENSITY = 0.1
FLOOR_ILLUM = 1.0
EPSILON = 1e-06

def dft_tables(length):
    pixel_index = jnp.arange(length, dtype=jnp.int32)
    product = pixel_index[:, None] * pixel_index[None, :] % length
    phase_angle = product.astype(jnp.float32) * (2.0 * math.pi / length)
    norm_scale = 1.0 / math.sqrt(length)
    return ((jnp.cos(phase_angle) * norm_scale).astype(jnp.bfloat16), (-jnp.sin(phase_angle) * norm_scale).astype(jnp.bfloat16))

def forward_pass(wave_re, wave_im, cos_t, sin_t):
    wave_re = wave_re.astype(jnp.float32)
    wave_im = wave_im.astype(jnp.float32)
    mid_re = (jnp.einsum('nab,bc->nac', wave_re, cos_t) - jnp.einsum('nab,bc->nac', wave_im, sin_t)).astype(jnp.bfloat16)
    mid_im = (jnp.einsum('nab,bc->nac', wave_re, sin_t) + jnp.einsum('nab,bc->nac', wave_im, cos_t)).astype(jnp.bfloat16)
    mid_re = mid_re.astype(jnp.float32)
    mid_im = mid_im.astype(jnp.float32)
    far_re = jnp.einsum('ab,nbc->nac', cos_t, mid_re) - jnp.einsum('ab,nbc->nac', sin_t, mid_im)
    far_im = jnp.einsum('ab,nbc->nac', sin_t, mid_re) + jnp.einsum('ab,nbc->nac', cos_t, mid_im)
    return (far_re, far_im)

def inverse_pass(spec_re, spec_im, cos_t, sin_t):
    spec_re = spec_re.astype(jnp.float32)
    spec_im = spec_im.astype(jnp.float32)
    half_re = (jnp.einsum('nab,bc->nac', spec_re, cos_t) + jnp.einsum('nab,bc->nac', spec_im, sin_t)).astype(jnp.bfloat16)
    half_im = (jnp.einsum('nab,bc->nac', spec_im, cos_t) - jnp.einsum('nab,bc->nac', spec_re, sin_t)).astype(jnp.bfloat16)
    half_re = half_re.astype(jnp.float32)
    half_im = half_im.astype(jnp.float32)
    back_re = jnp.einsum('ab,nbc->nac', cos_t, half_re) + jnp.einsum('ab,nbc->nac', sin_t, half_im)
    back_im = jnp.einsum('ab,nbc->nac', cos_t, half_im) - jnp.einsum('ab,nbc->nac', sin_t, half_re)
    return (back_re, back_im)

def highest_dot(left, right):
    return jnp.dot(left, right, precision=lax.Precision.HIGHEST, preferred_element_type=jnp.float32)

def gram_of(flat_re, flat_im):
    gram_re = highest_dot(flat_re, flat_re.T) + highest_dot(flat_im, flat_im.T)
    gram_im = highest_dot(flat_re, flat_im.T) - highest_dot(flat_im, flat_re.T)
    return (gram_re, gram_im)

def orthogonal_mix(gram_re, gram_im):
    mode_count = gram_re.shape[0]
    mode_power = jnp.diagonal(gram_re) + EPSILON
    inv_root = 1.0 / jnp.sqrt(mode_power)
    scale_mat = inv_root[:, None] * inv_root[None, :]
    norm_re = gram_re * scale_mat
    norm_im = gram_im * scale_mat
    embedded = jnp.concatenate([jnp.concatenate([norm_re, -norm_im], axis=1), jnp.concatenate([norm_im, norm_re], axis=1)], axis=0)
    frobenius = jnp.sqrt(jnp.sum(embedded * embedded))
    identity_mat = jnp.eye(2 * mode_count, dtype=jnp.float32)
    iterate_y = embedded / frobenius
    iterate_z = identity_mat
    for sweep_index in range(NS_ITERS):
        correction = 1.5 * identity_mat - 0.5 * highest_dot(iterate_z, iterate_y)
        iterate_y = highest_dot(iterate_y, correction)
        iterate_z = highest_dot(correction, iterate_z)
    root_inv = iterate_z / jnp.sqrt(frobenius)
    weight_re = root_inv[:mode_count, :mode_count]
    weight_im = root_inv[mode_count:, :mode_count]
    ratio_mat = inv_root[:, None] * jnp.sqrt(mode_power)[None, :]
    return (weight_re * ratio_mat, weight_im * ratio_mat)

def reference(object_field, probe_modes, scan_offsets, measured):
    cos_b, sin_b = dft_tables(M)
    cos_t = cos_b.astype(jnp.float32)
    sin_t = sin_b.astype(jnp.float32)
    probe_re = probe_modes[0]
    probe_im = probe_modes[1]
    illum_patch = lax.optimization_barrier(jnp.sum(probe_re * probe_re + probe_im * probe_im, axis=0))
    zero_index = jnp.zeros((), jnp.int32)

    def visit_position(state_carry, position):
        grad_re, grad_im, obj_norm, obj_terms = state_carry
        row_start = position // J_SC * TILE_R + scan_offsets[0, position]
        col_start = scan_offsets[1, position]
        obj_patch = lax.dynamic_slice(object_field, (zero_index, row_start, col_start), (2, M, M))
        obj_re = obj_patch[0]
        obj_im = obj_patch[1]
        wave_re = (probe_re * obj_re - probe_im * obj_im).astype(jnp.bfloat16)
        wave_im = (probe_re * obj_im + probe_im * obj_re).astype(jnp.bfloat16)
        far_re, far_im = forward_pass(wave_re, wave_im, cos_t, sin_t)
        intensity = lax.optimization_barrier(jnp.sum(far_re * far_re + far_im * far_im, axis=0))
        amp_ratio = jnp.sqrt(measured[position] / jnp.maximum(intensity, FLOOR_INTENSITY))
        factor = amp_ratio - 1.0
        spec_re = (factor * far_re).astype(jnp.bfloat16)
        spec_im = (factor * far_im).astype(jnp.bfloat16)
        back_re, back_im = inverse_pass(spec_re, spec_im, cos_t, sin_t)
        grad_re = grad_re + obj_re * back_re + obj_im * back_im
        grad_im = grad_im + obj_re * back_im - obj_im * back_re
        obj_norm = obj_norm + obj_re * obj_re + obj_im * obj_im
        patch_re = lax.optimization_barrier(jnp.sum(probe_re * back_re + probe_im * back_im, axis=0))
        patch_im = lax.optimization_barrier(jnp.sum(probe_re * back_im - probe_im * back_re, axis=0))
        patch_terms = jnp.stack([patch_re, patch_im, illum_patch])
        current = lax.dynamic_slice(obj_terms, (zero_index, row_start, col_start), (3, M, M))
        obj_terms = lax.dynamic_update_slice(obj_terms, current + patch_terms, (zero_index, row_start, col_start))
        return ((grad_re, grad_im, obj_norm, obj_terms), None)
    start_carry = (jnp.zeros((K, M, M), jnp.float32), jnp.zeros((K, M, M), jnp.float32), jnp.zeros((M, M), jnp.float32), jnp.zeros((3, OBJ_R, OBJ_C), jnp.float32))
    final_carry, unused = lax.scan(visit_position, start_carry, jnp.arange(J, dtype=jnp.int32))
    grad_re, grad_im, obj_norm, obj_terms = final_carry
    object_new = object_field + obj_terms[0:2] / jnp.maximum(obj_terms[2:3], FLOOR_ILLUM)
    step_re = (probe_re + grad_re / (obj_norm + EPSILON)).reshape(K, M * M)
    step_im = (probe_im + grad_im / (obj_norm + EPSILON)).reshape(K, M * M)
    gram_re, gram_im = gram_of(step_re, step_im)
    mix_re, mix_im = orthogonal_mix(gram_re, gram_im)
    new_re = highest_dot(mix_re.T, step_re) - highest_dot(mix_im.T, step_im)
    new_im = highest_dot(mix_re.T, step_im) + highest_dot(mix_im.T, step_re)
    probe_new = jnp.stack([new_re, new_im]).reshape(2, K, M, M)
    return (object_new, probe_new)
```

```python
import math

import jax
import jax.numpy as jnp
from jax import lax
from jax.sharding import PartitionSpec as P

M = 128
NS_ITERS = 8


FLOOR_INTENSITY = 0.1
FLOOR_ILLUM = 1.0
EPSILON = 1e-06


def dft_tables(length):
    pixel_index = jnp.arange(length, dtype=jnp.int32)
    product = pixel_index[:, None] * pixel_index[None, :] % length
    phase_angle = product.astype(jnp.float32) * (2.0 * math.pi / length)
    norm_scale = 1.0 / math.sqrt(length)
    return (
        (jnp.cos(phase_angle) * norm_scale).astype(jnp.bfloat16),
        (-jnp.sin(phase_angle) * norm_scale).astype(jnp.bfloat16),
    )


def right_product(left, table):
    return jnp.einsum("nab,bc->nac", left, table, preferred_element_type=jnp.float32)


def left_product(table, right):
    return jnp.einsum("ab,nbc->nac", table, right, preferred_element_type=jnp.float32)


def forward_pass(wave_re, wave_im, cos_t, sin_t):
    mid_re = (right_product(wave_re, cos_t) - right_product(wave_im, sin_t)).astype(jnp.bfloat16)
    mid_im = (right_product(wave_re, sin_t) + right_product(wave_im, cos_t)).astype(jnp.bfloat16)
    far_re = left_product(cos_t, mid_re) - left_product(sin_t, mid_im)
    far_im = left_product(sin_t, mid_re) + left_product(cos_t, mid_im)
    return (far_re, far_im)


def inverse_pass(spec_re, spec_im, cos_t, sin_t):
    half_re = (right_product(spec_re, cos_t) + right_product(spec_im, sin_t)).astype(jnp.bfloat16)
    half_im = (right_product(spec_im, cos_t) - right_product(spec_re, sin_t)).astype(jnp.bfloat16)
    back_re = left_product(cos_t, half_re) + left_product(sin_t, half_im)
    back_im = left_product(cos_t, half_im) - left_product(sin_t, half_re)
    return (back_re, back_im)


def highest_dot(left, right):
    return jnp.dot(left, right, precision=lax.Precision.HIGHEST, preferred_element_type=jnp.float32)


def gram_of(flat_re, flat_im):
    gram_re = highest_dot(flat_re, flat_re.T) + highest_dot(flat_im, flat_im.T)
    gram_im = highest_dot(flat_re, flat_im.T) - highest_dot(flat_im, flat_re.T)
    return (gram_re, gram_im)


def orthogonal_mix(gram_re, gram_im):
    mode_count = gram_re.shape[0]
    mode_power = jnp.diagonal(gram_re) + EPSILON
    inv_root = 1.0 / jnp.sqrt(mode_power)
    scale_mat = inv_root[:, None] * inv_root[None, :]
    norm_re = gram_re * scale_mat
    norm_im = gram_im * scale_mat
    embedded = jnp.concatenate(
        [jnp.concatenate([norm_re, -norm_im], axis=1), jnp.concatenate([norm_im, norm_re], axis=1)],
        axis=0,
    )
    frobenius = jnp.sqrt(jnp.sum(embedded * embedded))
    identity_mat = jnp.eye(2 * mode_count, dtype=jnp.float32)
    iterate_y = embedded / frobenius
    iterate_z = identity_mat
    for sweep_index in range(NS_ITERS):
        correction = 1.5 * identity_mat - 0.5 * highest_dot(iterate_z, iterate_y)
        iterate_y = highest_dot(iterate_y, correction)
        iterate_z = highest_dot(correction, iterate_z)
    root_inv = iterate_z / jnp.sqrt(frobenius)
    weight_re = root_inv[:mode_count, :mode_count]
    weight_im = root_inv[mode_count:, :mode_count]
    ratio_mat = inv_root[:, None] * jnp.sqrt(mode_power)[None, :]
    return (weight_re * ratio_mat, weight_im * ratio_mat)


def onehot_place(starts, out_len, in_len):
    out_index = jnp.arange(out_len, dtype=jnp.int32)[None, :, None]
    in_index = jnp.arange(in_len, dtype=jnp.int32)[None, None, :]
    return (out_index == starts[:, None, None] + in_index).astype(jnp.bfloat16)


def split_parts(values):
    high = values.astype(jnp.bfloat16)
    rest = values - high.astype(jnp.float32)
    middle = rest.astype(jnp.bfloat16)
    low = (rest - middle.astype(jnp.float32)).astype(jnp.bfloat16)
    return jnp.stack([high, middle, low])


def shards(object_field, probe_modes, scan_offsets, measured):
    mode_index = lax.axis_index("mode")
    cos_t, sin_t = dft_tables(M)
    probe_re = probe_modes[0, 0]
    probe_im = probe_modes[1, 0]
    row_starts = scan_offsets[0]
    col_starts = scan_offsets[1]
    local_count = row_starts.shape[0]
    zero_index = jnp.zeros((), jnp.int32)

    def cut_patch(row_start, col_start):
        return lax.dynamic_slice(object_field, (zero_index, row_start, col_start), (2, M, M))

    obj_patches = jax.vmap(cut_patch)(row_starts, col_starts)
    obj_re = obj_patches[:, 0]
    obj_im = obj_patches[:, 1]
    obj_norm = jnp.sum(obj_re * obj_re + obj_im * obj_im, axis=0)
    wave_re = (probe_re * obj_re - probe_im * obj_im).astype(jnp.bfloat16)
    wave_im = (probe_re * obj_im + probe_im * obj_re).astype(jnp.bfloat16)
    far_re, far_im = forward_pass(wave_re, wave_im, cos_t, sin_t)
    mode_intensity = far_re * far_re + far_im * far_im
    own_light = (probe_re * probe_re + probe_im * probe_im)[None]
    summed = lax.psum(jnp.concatenate([mode_intensity, own_light]), "mode")
    intensity = summed[:local_count]
    light_patch = summed[local_count:]
    amp_ratio = jnp.sqrt(measured / jnp.maximum(intensity, FLOOR_INTENSITY))
    factor = amp_ratio - 1.0
    spec_re = (factor * far_re).astype(jnp.bfloat16)
    spec_im = (factor * far_im).astype(jnp.bfloat16)
    back_re, back_im = inverse_pass(spec_re, spec_im, cos_t, sin_t)
    grad_re = jnp.sum(obj_re * back_re + obj_im * back_im, axis=0)
    grad_im = jnp.sum(obj_re * back_im - obj_im * back_re, axis=0)
    patch_re = probe_re * back_re + probe_im * back_im
    patch_im = probe_re * back_im - probe_im * back_re
    grad_re, grad_im, obj_norm = lax.psum((grad_re, grad_im, obj_norm), "scan")
    step_re = probe_re + grad_re / (obj_norm + EPSILON)
    step_im = probe_im + grad_im / (obj_norm + EPSILON)

    rows_share = object_field.shape[1] // lax.axis_size("mode")
    col_place = onehot_place(col_starts, object_field.shape[2], M)
    row_place = onehot_place(row_starts, object_field.shape[1], M)
    patch_parts = split_parts(jnp.stack([patch_re, patch_im]))
    placed_rows = jnp.einsum(
        "jia,pcjab->pcjib", row_place, patch_parts, preferred_element_type=jnp.float32
    ).astype(jnp.bfloat16)
    grad_tile = jnp.einsum(
        "pcjib,jkb->pcik", placed_rows, col_place, preferred_element_type=jnp.float32
    ).sum(axis=0)
    own_place = onehot_place(row_starts - mode_index * rows_share, rows_share, M)
    light_parts = split_parts(light_patch[0])
    light_rows = jnp.einsum(
        "jia,pab->pjib", own_place, light_parts, preferred_element_type=jnp.float32
    ).astype(jnp.bfloat16)
    light_rows = jnp.einsum(
        "pjib,jkb->pik", light_rows, col_place, preferred_element_type=jnp.float32
    ).sum(axis=0)[None]
    grad_rows = lax.psum_scatter(grad_tile, "mode", scatter_dimension=1, tiled=True)
    own_rows = lax.dynamic_slice_in_dim(object_field, mode_index * rows_share, rows_share, 1)
    object_new = own_rows + grad_rows / jnp.maximum(light_rows, FLOOR_ILLUM)
    flat_mine = jnp.stack([step_re.reshape(-1), step_im.reshape(-1)])[:, None, :]
    every_mode = lax.all_gather(flat_mine, "mode", axis=1, tiled=True)
    gathered_re = every_mode[0]
    gathered_im = every_mode[1]
    gram_re, gram_im = gram_of(gathered_re, gathered_im)
    mix_re, mix_im = orthogonal_mix(gram_re, gram_im)
    column_re = lax.dynamic_slice_in_dim(mix_re, mode_index, 1, 1)
    column_im = lax.dynamic_slice_in_dim(mix_im, mode_index, 1, 1)
    mine_re = highest_dot(column_re.T, gathered_re) - highest_dot(column_im.T, gathered_im)
    mine_im = highest_dot(column_re.T, gathered_im) + highest_dot(column_im.T, gathered_re)
    mine = jnp.stack([mine_re, mine_im])
    probe_new = mine.reshape(2, 1, M, M)
    return (object_new, probe_new)


def solution(mesh):
    placed = (
        P(None, "scan", None),
        P(None, "mode", None, None),
        P(None, "scan"),
        P("scan", None, None),
    )
    return jax.shard_map(
        shards,
        mesh=mesh,
        in_specs=placed,
        out_specs=(P(None, ("scan", "mode"), None), P(None, "mode", None, None)),
        check_vma=False,
    )
```

```python
import math

import jax
import jax.numpy as jnp
from jax import lax
from jax.sharding import PartitionSpec as P

M = 128
NS_ITERS = 8


FLOOR_INTENSITY = 0.1
FLOOR_ILLUM = 1.0
EPSILON = 1e-06


def dft_tables(length):
    pixel_index = jnp.arange(length, dtype=jnp.int32)
    product = pixel_index[:, None] * pixel_index[None, :] % length
    phase_angle = product.astype(jnp.float32) * (2.0 * math.pi / length)
    norm_scale = 1.0 / math.sqrt(length)
    return (
        (jnp.cos(phase_angle) * norm_scale).astype(jnp.bfloat16),
        (-jnp.sin(phase_angle) * norm_scale).astype(jnp.bfloat16),
    )


def right_product(left, table):
    return jnp.einsum("nab,bc->nac", left, table, preferred_element_type=jnp.float32)


def left_product(table, right):
    return jnp.einsum("ab,nbc->nac", table, right, preferred_element_type=jnp.float32)


def forward_pass(wave_re, wave_im, cos_t, sin_t):
    mid_re = (right_product(wave_re, cos_t) - right_product(wave_im, sin_t)).astype(jnp.bfloat16)
    mid_im = (right_product(wave_re, sin_t) + right_product(wave_im, cos_t)).astype(jnp.bfloat16)
    far_re = left_product(cos_t, mid_re) - left_product(sin_t, mid_im)
    far_im = left_product(sin_t, mid_re) + left_product(cos_t, mid_im)
    return (far_re, far_im)


def inverse_pass(spec_re, spec_im, cos_t, sin_t):
    half_re = (right_product(spec_re, cos_t) + right_product(spec_im, sin_t)).astype(jnp.bfloat16)
    half_im = (right_product(spec_im, cos_t) - right_product(spec_re, sin_t)).astype(jnp.bfloat16)
    back_re = left_product(cos_t, half_re) + left_product(sin_t, half_im)
    back_im = left_product(cos_t, half_im) - left_product(sin_t, half_re)
    return (back_re, back_im)


def highest_dot(left, right):
    return jnp.dot(left, right, precision=lax.Precision.HIGHEST, preferred_element_type=jnp.float32)


def gram_of(flat_re, flat_im):
    gram_re = highest_dot(flat_re, flat_re.T) + highest_dot(flat_im, flat_im.T)
    gram_im = highest_dot(flat_re, flat_im.T) - highest_dot(flat_im, flat_re.T)
    return (gram_re, gram_im)


def orthogonal_mix(gram_re, gram_im):
    mode_count = gram_re.shape[0]
    mode_power = jnp.diagonal(gram_re) + EPSILON
    inv_root = 1.0 / jnp.sqrt(mode_power)
    scale_mat = inv_root[:, None] * inv_root[None, :]
    norm_re = gram_re * scale_mat
    norm_im = gram_im * scale_mat
    embedded = jnp.concatenate(
        [jnp.concatenate([norm_re, -norm_im], axis=1), jnp.concatenate([norm_im, norm_re], axis=1)],
        axis=0,
    )
    frobenius = jnp.sqrt(jnp.sum(embedded * embedded))
    identity_mat = jnp.eye(2 * mode_count, dtype=jnp.float32)
    iterate_y = embedded / frobenius
    iterate_z = identity_mat
    for sweep_index in range(NS_ITERS):
        correction = 1.5 * identity_mat - 0.5 * highest_dot(iterate_z, iterate_y)
        iterate_y = highest_dot(iterate_y, correction)
        iterate_z = highest_dot(correction, iterate_z)
    root_inv = iterate_z / jnp.sqrt(frobenius)
    weight_re = root_inv[:mode_count, :mode_count]
    weight_im = root_inv[mode_count:, :mode_count]
    ratio_mat = inv_root[:, None] * jnp.sqrt(mode_power)[None, :]
    return (weight_re * ratio_mat, weight_im * ratio_mat)


def onehot_place(starts, out_len, in_len):
    out_index = jnp.arange(out_len, dtype=jnp.int32)[None, :, None]
    in_index = jnp.arange(in_len, dtype=jnp.int32)[None, None, :]
    return (out_index == starts[:, None, None] + in_index).astype(jnp.bfloat16)


def split_parts(values):
    high = values.astype(jnp.bfloat16)
    rest = values - high.astype(jnp.float32)
    middle = rest.astype(jnp.bfloat16)
    low = (rest - middle.astype(jnp.float32)).astype(jnp.bfloat16)
    return jnp.stack([high, middle, low])


def shards(object_field, probe_modes, scan_offsets, measured):
    mode_index = lax.axis_index("mode")
    cos_t, sin_t = dft_tables(M)
    probe_re = probe_modes[0, 0]
    probe_im = probe_modes[1, 0]
    row_starts = scan_offsets[0]
    col_starts = scan_offsets[1]
    local_count = row_starts.shape[0]

    col_place = onehot_place(col_starts, object_field.shape[2], M)
    row_place = onehot_place(row_starts, object_field.shape[1], M)
    field_parts = split_parts(object_field)
    picked_cols = jnp.einsum(
        "pcik,jkb->pcijb", field_parts, col_place, preferred_element_type=jnp.float32
    ).astype(jnp.bfloat16)
    obj_patches = jnp.einsum(
        "jia,pcijb->pcjab", row_place, picked_cols, preferred_element_type=jnp.float32
    ).sum(axis=0)
    obj_re = obj_patches[0]
    obj_im = obj_patches[1]
    obj_norm = jnp.sum(obj_re * obj_re + obj_im * obj_im, axis=0)
    wave_re = (probe_re * obj_re - probe_im * obj_im).astype(jnp.bfloat16)
    wave_im = (probe_re * obj_im + probe_im * obj_re).astype(jnp.bfloat16)
    far_re, far_im = forward_pass(wave_re, wave_im, cos_t, sin_t)
    mode_intensity = far_re * far_re + far_im * far_im
    own_light = (probe_re * probe_re + probe_im * probe_im)[None]
    summed = lax.psum(jnp.concatenate([mode_intensity, own_light]), "mode")
    intensity = summed[:local_count]
    light_patch = summed[local_count:]
    amp_ratio = jnp.sqrt(measured / jnp.maximum(intensity, FLOOR_INTENSITY))
    factor = amp_ratio - 1.0
    spec_re = (factor * far_re).astype(jnp.bfloat16)
    spec_im = (factor * far_im).astype(jnp.bfloat16)
    back_re, back_im = inverse_pass(spec_re, spec_im, cos_t, sin_t)
    grad_re = jnp.sum(obj_re * back_re + obj_im * back_im, axis=0)
    grad_im = jnp.sum(obj_re * back_im - obj_im * back_re, axis=0)
    patch_re = probe_re * back_re + probe_im * back_im
    patch_im = probe_re * back_im - probe_im * back_re
    grad_re, grad_im, obj_norm = lax.psum((grad_re, grad_im, obj_norm), "scan")
    step_re = probe_re + grad_re / (obj_norm + EPSILON)
    step_im = probe_im + grad_im / (obj_norm + EPSILON)

    rows_share = object_field.shape[1] // lax.axis_size("mode")
    patch_parts = split_parts(jnp.stack([patch_re, patch_im]))
    placed_rows = jnp.einsum(
        "jia,pcjab->pcjib", row_place, patch_parts, preferred_element_type=jnp.float32
    ).astype(jnp.bfloat16)
    grad_tile = jnp.einsum(
        "pcjib,jkb->pcik", placed_rows, col_place, preferred_element_type=jnp.float32
    ).sum(axis=0)
    own_place = onehot_place(row_starts - mode_index * rows_share, rows_share, M)
    light_parts = split_parts(light_patch[0])
    light_rows = jnp.einsum(
        "jia,pab->pjib", own_place, light_parts, preferred_element_type=jnp.float32
    ).astype(jnp.bfloat16)
    light_rows = jnp.einsum(
        "pjib,jkb->pik", light_rows, col_place, preferred_element_type=jnp.float32
    ).sum(axis=0)[None]
    own_rows = lax.dynamic_slice_in_dim(object_field, mode_index * rows_share, rows_share, 1)
    flat_mine = jnp.stack([step_re.reshape(-1), step_im.reshape(-1)])[:, None, :]
    every_mode = lax.all_gather(flat_mine, "mode", axis=1, tiled=True)
    mode_count = lax.axis_size("mode")
    grad_blocks = grad_tile.reshape(2, mode_count, rows_share, grad_tile.shape[2])
    grad_rows = lax.all_to_all(grad_blocks, "mode", 1, 1, tiled=False).sum(axis=1)
    object_new = own_rows + grad_rows / jnp.maximum(light_rows, FLOOR_ILLUM)
    gathered_re = every_mode[0]
    gathered_im = every_mode[1]
    gram_re, gram_im = gram_of(gathered_re, gathered_im)
    mix_re, mix_im = orthogonal_mix(gram_re, gram_im)
    column_re = lax.dynamic_slice_in_dim(mix_re, mode_index, 1, 1)
    column_im = lax.dynamic_slice_in_dim(mix_im, mode_index, 1, 1)
    mine_re = highest_dot(column_re.T, gathered_re) - highest_dot(column_im.T, gathered_im)
    mine_im = highest_dot(column_re.T, gathered_im) + highest_dot(column_im.T, gathered_re)
    mine = jnp.stack([mine_re, mine_im])
    probe_new = mine.reshape(2, 1, M, M)
    return (object_new, probe_new)


def solution(mesh):
    placed = (
        P(None, "scan", None),
        P(None, "mode", None, None),
        P(None, "scan"),
        P("scan", None, None),
    )
    return jax.shard_map(
        shards,
        mesh=mesh,
        in_specs=placed,
        out_specs=(P(None, ("scan", "mode"), None), P(None, "mode", None, None)),
        check_vma=False,
    )
```

```python
import math

import jax
import jax.numpy as jnp
from jax import lax
from jax.sharding import PartitionSpec as P

M = 128
NS_ITERS = 8


FLOOR_INTENSITY = 0.1
FLOOR_ILLUM = 1.0
EPSILON = 1e-06


def dft_tables(length):
    pixel_index = jnp.arange(length, dtype=jnp.int32)
    product = pixel_index[:, None] * pixel_index[None, :] % length
    phase_angle = product.astype(jnp.float32) * (2.0 * math.pi / length)
    norm_scale = 1.0 / math.sqrt(length)
    return (
        (jnp.cos(phase_angle) * norm_scale).astype(jnp.bfloat16),
        (-jnp.sin(phase_angle) * norm_scale).astype(jnp.bfloat16),
    )


def right_product(left, table):
    return jnp.einsum("nab,bc->nac", left, table, preferred_element_type=jnp.float32)


def left_product(table, right):
    return jnp.einsum("ab,nbc->nac", table, right, preferred_element_type=jnp.float32)


def forward_pass(wave_re, wave_im, cos_t, sin_t):
    mid_re = (right_product(wave_re, cos_t) - right_product(wave_im, sin_t)).astype(jnp.bfloat16)
    mid_im = (right_product(wave_re, sin_t) + right_product(wave_im, cos_t)).astype(jnp.bfloat16)
    far_re = left_product(cos_t, mid_re) - left_product(sin_t, mid_im)
    far_im = left_product(sin_t, mid_re) + left_product(cos_t, mid_im)
    return (far_re, far_im)


def inverse_pass(spec_re, spec_im, cos_t, sin_t):
    half_re = (right_product(spec_re, cos_t) + right_product(spec_im, sin_t)).astype(jnp.bfloat16)
    half_im = (right_product(spec_im, cos_t) - right_product(spec_re, sin_t)).astype(jnp.bfloat16)
    back_re = left_product(cos_t, half_re) + left_product(sin_t, half_im)
    back_im = left_product(cos_t, half_im) - left_product(sin_t, half_re)
    return (back_re, back_im)


def highest_dot(left, right):
    return jnp.dot(left, right, precision=lax.Precision.HIGHEST, preferred_element_type=jnp.float32)


def gram_of(flat_re, flat_im):
    gram_re = highest_dot(flat_re, flat_re.T) + highest_dot(flat_im, flat_im.T)
    gram_im = highest_dot(flat_re, flat_im.T) - highest_dot(flat_im, flat_re.T)
    return (gram_re, gram_im)


def orthogonal_mix(gram_re, gram_im):
    mode_count = gram_re.shape[0]
    mode_power = jnp.diagonal(gram_re) + EPSILON
    inv_root = 1.0 / jnp.sqrt(mode_power)
    scale_mat = inv_root[:, None] * inv_root[None, :]
    norm_re = gram_re * scale_mat
    norm_im = gram_im * scale_mat
    embedded = jnp.concatenate(
        [jnp.concatenate([norm_re, -norm_im], axis=1), jnp.concatenate([norm_im, norm_re], axis=1)],
        axis=0,
    )
    frobenius = jnp.sqrt(jnp.sum(embedded * embedded))
    identity_mat = jnp.eye(2 * mode_count, dtype=jnp.float32)
    iterate_y = embedded / frobenius
    iterate_z = identity_mat
    for sweep_index in range(NS_ITERS):
        correction = 1.5 * identity_mat - 0.5 * highest_dot(iterate_z, iterate_y)
        iterate_y = highest_dot(iterate_y, correction)
        iterate_z = highest_dot(correction, iterate_z)
    root_inv = iterate_z / jnp.sqrt(frobenius)
    weight_re = root_inv[:mode_count, :mode_count]
    weight_im = root_inv[mode_count:, :mode_count]
    ratio_mat = inv_root[:, None] * jnp.sqrt(mode_power)[None, :]
    return (weight_re * ratio_mat, weight_im * ratio_mat)


def onehot_place(starts, out_len, in_len):
    out_index = jnp.arange(out_len, dtype=jnp.int32)[None, :, None]
    in_index = jnp.arange(in_len, dtype=jnp.int32)[None, None, :]
    return (out_index == starts[:, None, None] + in_index).astype(jnp.bfloat16)


def split_parts(values):
    high = values.astype(jnp.bfloat16)
    rest = values - high.astype(jnp.float32)
    middle = rest.astype(jnp.bfloat16)
    low = (rest - middle.astype(jnp.float32)).astype(jnp.bfloat16)
    return jnp.stack([high, middle, low])


def exchange_sum(values, axis_name):
    count = lax.axis_size(axis_name)
    pieces = values.reshape(count, -1)
    mine = lax.all_to_all(pieces, axis_name, 0, 0, tiled=False).sum(axis=0)
    spread = jnp.broadcast_to(mine[None], pieces.shape)
    return lax.all_to_all(spread, axis_name, 0, 0, tiled=False).reshape(values.shape)


def shards(object_field, probe_modes, scan_offsets, measured):
    mode_index = lax.axis_index("mode")
    cos_t, sin_t = dft_tables(M)
    probe_re = probe_modes[0, 0]
    probe_im = probe_modes[1, 0]
    row_starts = scan_offsets[0]
    col_starts = scan_offsets[1]
    local_count = row_starts.shape[0]

    col_place = onehot_place(col_starts, object_field.shape[2], M)
    row_place = onehot_place(row_starts, object_field.shape[1], M)
    field_parts = split_parts(object_field)
    picked_cols = jnp.einsum(
        "pcik,jkb->pcijb", field_parts, col_place, preferred_element_type=jnp.float32
    ).astype(jnp.bfloat16)
    obj_patches = jnp.einsum(
        "jia,pcijb->pcjab", row_place, picked_cols, preferred_element_type=jnp.float32
    ).sum(axis=0)
    obj_re = obj_patches[0]
    obj_im = obj_patches[1]
    obj_norm = jnp.sum(obj_re * obj_re + obj_im * obj_im, axis=0)
    wave_re = (probe_re * obj_re - probe_im * obj_im).astype(jnp.bfloat16)
    wave_im = (probe_re * obj_im + probe_im * obj_re).astype(jnp.bfloat16)
    far_re, far_im = forward_pass(wave_re, wave_im, cos_t, sin_t)
    mode_intensity = far_re * far_re + far_im * far_im
    own_light = (probe_re * probe_re + probe_im * probe_im)[None]
    summed = exchange_sum(jnp.concatenate([mode_intensity, own_light]), "mode")
    intensity = summed[:local_count]
    light_patch = summed[local_count:]
    amp_ratio = jnp.sqrt(measured / jnp.maximum(intensity, FLOOR_INTENSITY))
    factor = amp_ratio - 1.0
    spec_re = (factor * far_re).astype(jnp.bfloat16)
    spec_im = (factor * far_im).astype(jnp.bfloat16)
    back_re, back_im = inverse_pass(spec_re, spec_im, cos_t, sin_t)
    grad_re = jnp.sum(obj_re * back_re + obj_im * back_im, axis=0)
    grad_im = jnp.sum(obj_re * back_im - obj_im * back_re, axis=0)
    patch_re = probe_re * back_re + probe_im * back_im
    patch_im = probe_re * back_im - probe_im * back_re

    rows_share = object_field.shape[1] // lax.axis_size("mode")
    patch_parts = split_parts(jnp.stack([patch_re, patch_im]))
    placed_rows = jnp.einsum(
        "jia,pcjab->pcjib", row_place, patch_parts, preferred_element_type=jnp.float32
    ).astype(jnp.bfloat16)
    grad_tile = jnp.einsum(
        "pcjib,jkb->pcik", placed_rows, col_place, preferred_element_type=jnp.float32
    ).sum(axis=0)
    own_place = onehot_place(row_starts - mode_index * rows_share, rows_share, M)
    light_parts = split_parts(light_patch[0])
    light_rows = jnp.einsum(
        "jia,pab->pjib", own_place, light_parts, preferred_element_type=jnp.float32
    ).astype(jnp.bfloat16)
    light_rows = jnp.einsum(
        "pjib,jkb->pik", light_rows, col_place, preferred_element_type=jnp.float32
    ).sum(axis=0)[None]
    own_rows = lax.dynamic_slice_in_dim(object_field, mode_index * rows_share, rows_share, 1)
    grad_sums = jnp.stack([grad_re, grad_im, obj_norm])
    grad_sums, grad_tile = lax.optimization_barrier((grad_sums, grad_tile))
    grad_sums = exchange_sum(grad_sums, "scan")
    step_re = probe_re + grad_sums[0] / (grad_sums[2] + EPSILON)
    step_im = probe_im + grad_sums[1] / (grad_sums[2] + EPSILON)
    flat_mine = jnp.stack([step_re.reshape(-1), step_im.reshape(-1)])[:, None, :]
    every_mode = lax.all_gather(flat_mine, "mode", axis=1, tiled=True)
    mode_count = lax.axis_size("mode")
    grad_blocks = grad_tile.reshape(2, mode_count, rows_share, grad_tile.shape[2])
    grad_rows = lax.all_to_all(grad_blocks, "mode", 1, 1, tiled=False).sum(axis=1)
    object_new = own_rows + grad_rows / jnp.maximum(light_rows, FLOOR_ILLUM)
    gathered_re = every_mode[0]
    gathered_im = every_mode[1]
    gram_re, gram_im = gram_of(gathered_re, gathered_im)
    mix_re, mix_im = orthogonal_mix(gram_re, gram_im)
    column_re = lax.dynamic_slice_in_dim(mix_re, mode_index, 1, 1)
    column_im = lax.dynamic_slice_in_dim(mix_im, mode_index, 1, 1)
    mine_re = highest_dot(column_re.T, gathered_re) - highest_dot(column_im.T, gathered_im)
    mine_im = highest_dot(column_re.T, gathered_im) + highest_dot(column_im.T, gathered_re)
    mine = jnp.stack([mine_re, mine_im])
    probe_new = mine.reshape(2, 1, M, M)
    return (object_new, probe_new)


def solution(mesh):
    placed = (
        P(None, "scan", None),
        P(None, "mode", None, None),
        P(None, "scan"),
        P("scan", None, None),
    )
    return jax.shard_map(
        shards,
        mesh=mesh,
        in_specs=placed,
        out_specs=(P(None, ("scan", "mode"), None), P(None, "mode", None, None)),
        check_vma=False,
    )
```

```python
import math

import jax
import jax.numpy as jnp
from jax import lax
from jax.sharding import PartitionSpec as P

M = 128
NS_ITERS = 8


FLOOR_INTENSITY = 0.1
FLOOR_ILLUM = 1.0
EPSILON = 1e-06


def dft_tables(length):
    pixel_index = jnp.arange(length, dtype=jnp.int32)
    product = pixel_index[:, None] * pixel_index[None, :] % length
    phase_angle = product.astype(jnp.float32) * (2.0 * math.pi / length)
    norm_scale = 1.0 / math.sqrt(length)
    return (
        (jnp.cos(phase_angle) * norm_scale).astype(jnp.bfloat16),
        (-jnp.sin(phase_angle) * norm_scale).astype(jnp.bfloat16),
    )


def right_product(left, table):
    return jnp.einsum("nab,bc->nac", left, table, preferred_element_type=jnp.float32)


def left_product(table, right):
    return jnp.einsum("ab,nbc->nac", table, right, preferred_element_type=jnp.float32)


def forward_pass(wave_re, wave_im, cos_t, sin_t):
    mid_re = (right_product(wave_re, cos_t) - right_product(wave_im, sin_t)).astype(jnp.bfloat16)
    mid_im = (right_product(wave_re, sin_t) + right_product(wave_im, cos_t)).astype(jnp.bfloat16)
    far_re = left_product(cos_t, mid_re) - left_product(sin_t, mid_im)
    far_im = left_product(sin_t, mid_re) + left_product(cos_t, mid_im)
    return (far_re, far_im)


def inverse_pass(spec_re, spec_im, cos_t, sin_t):
    half_re = (right_product(spec_re, cos_t) + right_product(spec_im, sin_t)).astype(jnp.bfloat16)
    half_im = (right_product(spec_im, cos_t) - right_product(spec_re, sin_t)).astype(jnp.bfloat16)
    back_re = left_product(cos_t, half_re) + left_product(sin_t, half_im)
    back_im = left_product(cos_t, half_im) - left_product(sin_t, half_re)
    return (back_re, back_im)


def highest_dot(left, right):
    return jnp.dot(left, right, precision=lax.Precision.HIGHEST, preferred_element_type=jnp.float32)


def pixel_dot(left, right):
    return jnp.einsum(
        "kab,lab->kl", left, right,
        precision=lax.Precision.HIGHEST, preferred_element_type=jnp.float32,
    )


def mix_all(weights, modes):
    return jnp.einsum(
        "lk,lab->kab", weights, modes,
        precision=lax.Precision.HIGHEST, preferred_element_type=jnp.float32,
    )


def gram_of(modes_re, modes_im):
    gram_re = pixel_dot(modes_re, modes_re) + pixel_dot(modes_im, modes_im)
    gram_im = pixel_dot(modes_re, modes_im) - pixel_dot(modes_im, modes_re)
    return (gram_re, gram_im)


def orthogonal_mix(gram_re, gram_im):
    mode_count = gram_re.shape[0]
    mode_power = jnp.diagonal(gram_re) + EPSILON
    inv_root = 1.0 / jnp.sqrt(mode_power)
    scale_mat = inv_root[:, None] * inv_root[None, :]
    norm_re = gram_re * scale_mat
    norm_im = gram_im * scale_mat
    embedded = jnp.concatenate(
        [jnp.concatenate([norm_re, -norm_im], axis=1), jnp.concatenate([norm_im, norm_re], axis=1)],
        axis=0,
    )
    frobenius = jnp.sqrt(jnp.sum(embedded * embedded))
    identity_mat = jnp.eye(2 * mode_count, dtype=jnp.float32)
    iterate_y = embedded / frobenius
    iterate_z = identity_mat
    def sweep(sweep_index, iterates):
        iterate_y, iterate_z = iterates
        correction = 1.5 * identity_mat - 0.5 * highest_dot(iterate_z, iterate_y)
        return (highest_dot(iterate_y, correction), highest_dot(correction, iterate_z))

    iterate_y, iterate_z = lax.fori_loop(0, NS_ITERS, sweep, (iterate_y, iterate_z))
    root_inv = iterate_z / jnp.sqrt(frobenius)
    weight_re = root_inv[:mode_count, :mode_count]
    weight_im = root_inv[mode_count:, :mode_count]
    ratio_mat = inv_root[:, None] * jnp.sqrt(mode_power)[None, :]
    return (weight_re * ratio_mat, weight_im * ratio_mat)


def onehot_place(starts, out_len, in_len):
    out_index = jnp.arange(out_len, dtype=jnp.int32)[None, :, None]
    in_index = jnp.arange(in_len, dtype=jnp.int32)[None, None, :]
    return (out_index == starts[:, None, None] + in_index).astype(jnp.bfloat16)


def split_parts(values):
    high = values.astype(jnp.bfloat16)
    rest = values - high.astype(jnp.float32)
    middle = rest.astype(jnp.bfloat16)
    low = (rest - middle.astype(jnp.float32)).astype(jnp.bfloat16)
    return jnp.stack([high, middle, low])


def exchange_sum(values, axis_name):
    count = lax.axis_size(axis_name)
    pieces = values.reshape(count, -1)
    mine = lax.all_to_all(pieces, axis_name, 0, 0, tiled=False).sum(axis=0)
    spread = jnp.broadcast_to(mine[None], pieces.shape)
    return lax.all_to_all(spread, axis_name, 0, 0, tiled=False).reshape(values.shape)


def shards(object_field, probe_modes, scan_offsets, measured):
    mode_index = lax.axis_index("mode")
    cos_t, sin_t = dft_tables(M)
    probe_re = probe_modes[0, 0]
    probe_im = probe_modes[1, 0]
    row_starts = scan_offsets[0]
    col_starts = scan_offsets[1]
    local_count = row_starts.shape[0]

    col_place = onehot_place(col_starts, object_field.shape[2], M)
    row_place = onehot_place(row_starts, object_field.shape[1], M)
    field_parts = split_parts(object_field)
    picked_cols = jnp.einsum(
        "pcik,jkb->pcijb", field_parts, col_place, preferred_element_type=jnp.float32
    ).astype(jnp.bfloat16)
    obj_patches = jnp.einsum(
        "jia,pcijb->pcjab", row_place, picked_cols, preferred_element_type=jnp.float32
    ).sum(axis=0)
    obj_re = obj_patches[0]
    obj_im = obj_patches[1]
    obj_norm = jnp.sum(obj_re * obj_re + obj_im * obj_im, axis=0)
    wave_re = (probe_re * obj_re - probe_im * obj_im).astype(jnp.bfloat16)
    wave_im = (probe_re * obj_im + probe_im * obj_re).astype(jnp.bfloat16)
    far_re, far_im = forward_pass(wave_re, wave_im, cos_t, sin_t)
    mode_intensity = far_re * far_re + far_im * far_im
    own_light = (probe_re * probe_re + probe_im * probe_im)[None]
    summed = exchange_sum(jnp.concatenate([mode_intensity, own_light]), "mode")
    intensity = summed[:local_count]
    light_patch = summed[local_count:]
    amp_ratio = jnp.sqrt(measured / jnp.maximum(intensity, FLOOR_INTENSITY))
    factor = amp_ratio - 1.0
    spec_re = (factor * far_re).astype(jnp.bfloat16)
    spec_im = (factor * far_im).astype(jnp.bfloat16)
    back_re, back_im = inverse_pass(spec_re, spec_im, cos_t, sin_t)
    grad_re = jnp.sum(obj_re * back_re + obj_im * back_im, axis=0)
    grad_im = jnp.sum(obj_re * back_im - obj_im * back_re, axis=0)
    patch_re = probe_re * back_re + probe_im * back_im
    patch_im = probe_re * back_im - probe_im * back_re

    rows_share = object_field.shape[1] // lax.axis_size("mode")
    patch_parts = split_parts(jnp.stack([patch_re, patch_im]))
    placed_rows = jnp.einsum(
        "jia,pcjab->pcjib", row_place, patch_parts, preferred_element_type=jnp.float32
    ).astype(jnp.bfloat16)
    grad_tile = jnp.einsum(
        "pcjib,jkb->pcik", placed_rows, col_place, preferred_element_type=jnp.float32
    ).sum(axis=0)
    own_place = onehot_place(row_starts - mode_index * rows_share, rows_share, M)
    light_parts = split_parts(light_patch[0])
    light_rows = jnp.einsum(
        "jia,pab->pjib", own_place, light_parts, preferred_element_type=jnp.float32
    ).astype(jnp.bfloat16)
    light_rows = jnp.einsum(
        "pjib,jkb->pik", light_rows, col_place, preferred_element_type=jnp.float32
    ).sum(axis=0)[None]
    own_rows = lax.dynamic_slice_in_dim(object_field, mode_index * rows_share, rows_share, 1)
    scan_count = lax.axis_size("scan")
    scan_index = lax.axis_index("scan")
    chunk_rows = M // scan_count
    grad_sums = jnp.stack([grad_re, grad_im, obj_norm]).reshape(3, scan_count, chunk_rows, M)
    grad_sums, grad_tile = lax.optimization_barrier((grad_sums, grad_tile))
    mode_count = lax.axis_size("mode")
    grad_sums = lax.all_to_all(grad_sums, "scan", 1, 1, tiled=False).sum(axis=1)
    probe_rows = lax.dynamic_slice_in_dim(probe_modes[:, 0], scan_index * chunk_rows, chunk_rows, 1)
    step_rows = probe_rows + grad_sums[0:2] / (grad_sums[2] + EPSILON)
    grad_blocks = grad_tile.reshape(2, mode_count, -1)
    block_size = grad_blocks.shape[2]
    spread_rows = jnp.broadcast_to(step_rows.reshape(2, 1, -1), (2, mode_count, chunk_rows * M))
    received = lax.all_to_all(
        jnp.concatenate([grad_blocks, spread_rows], axis=2), "mode", 1, 1, tiled=False
    )
    grad_rows = received[:, :, :block_size].sum(axis=1).reshape(2, rows_share, grad_tile.shape[2])
    object_new = own_rows + grad_rows / jnp.maximum(light_rows, FLOOR_ILLUM)
    every_rows = received[:, :, block_size:].reshape(2, mode_count, chunk_rows, M)
    rows_re = every_rows[0]
    rows_im = every_rows[1]
    gram_re, gram_im = gram_of(rows_re, rows_im)
    gram_both = exchange_sum(jnp.stack([gram_re, gram_im]), "scan")
    mix_re, mix_im = orthogonal_mix(gram_both[0], gram_both[1])
    new_re = mix_all(mix_re, rows_re) - mix_all(mix_im, rows_im)
    new_im = mix_all(mix_re, rows_im) + mix_all(mix_im, rows_re)
    mine_rows = jnp.stack([
        lax.dynamic_index_in_dim(new_re, mode_index, 0, keepdims=False),
        lax.dynamic_index_in_dim(new_im, mode_index, 0, keepdims=False),
    ])
    spread_mine = jnp.broadcast_to(mine_rows[None], (scan_count,) + mine_rows.shape)
    all_rows = lax.all_to_all(spread_mine, "scan", 0, 0, tiled=False)
    probe_new = all_rows.transpose(1, 0, 2, 3).reshape(2, 1, M, M)
    return (object_new, probe_new)


def solution(mesh):
    placed = (
        P(None, "scan", None),
        P(None, "mode", None, None),
        P(None, "scan"),
        P("scan", None, None),
    )
    return jax.shard_map(
        shards,
        mesh=mesh,
        in_specs=placed,
        out_specs=(P(None, ("scan", "mode"), None), P(None, "mode", None, None)),
        check_vma=False,
    )
```

```python
import math

import jax
import jax.numpy as jnp
from jax import lax
from jax.sharding import PartitionSpec as P

M = 128
NS_ITERS = 8


FLOOR_INTENSITY = 0.1
FLOOR_ILLUM = 1.0
EPSILON = 1e-06


def dft_tables(length):
    pixel_index = jnp.arange(length, dtype=jnp.int32)
    product = pixel_index[:, None] * pixel_index[None, :] % length
    phase_angle = product.astype(jnp.float32) * (2.0 * math.pi / length)
    norm_scale = 1.0 / math.sqrt(length)
    return (
        (jnp.cos(phase_angle) * norm_scale).astype(jnp.bfloat16),
        (-jnp.sin(phase_angle) * norm_scale).astype(jnp.bfloat16),
    )


def right_product(left, table):
    return jnp.einsum("nab,bc->nac", left, table, preferred_element_type=jnp.float32)


def left_product(table, right):
    return jnp.einsum("ab,nbc->nac", table, right, preferred_element_type=jnp.float32)


def forward_pass(wave_re, wave_im, cos_t, sin_t):
    mid_re = (right_product(wave_re, cos_t) - right_product(wave_im, sin_t)).astype(jnp.bfloat16)
    mid_im = (right_product(wave_re, sin_t) + right_product(wave_im, cos_t)).astype(jnp.bfloat16)
    far_re = left_product(cos_t, mid_re) - left_product(sin_t, mid_im)
    far_im = left_product(sin_t, mid_re) + left_product(cos_t, mid_im)
    return (far_re, far_im)


def inverse_pass(spec_re, spec_im, cos_t, sin_t):
    half_re = (right_product(spec_re, cos_t) + right_product(spec_im, sin_t)).astype(jnp.bfloat16)
    half_im = (right_product(spec_im, cos_t) - right_product(spec_re, sin_t)).astype(jnp.bfloat16)
    back_re = left_product(cos_t, half_re) + left_product(sin_t, half_im)
    back_im = left_product(cos_t, half_im) - left_product(sin_t, half_re)
    return (back_re, back_im)


def highest_dot(left, right):
    return jnp.dot(left, right, precision=lax.Precision.HIGHEST, preferred_element_type=jnp.float32)


def pixel_dot(left, right):
    return jnp.einsum(
        "kab,lab->kl", left, right,
        precision=lax.Precision.HIGHEST, preferred_element_type=jnp.float32,
    )


def mix_all(weights, modes):
    return jnp.einsum(
        "lk,lab->kab", weights, modes,
        precision=lax.Precision.HIGHEST, preferred_element_type=jnp.float32,
    )


def gram_of(modes_re, modes_im):
    gram_re = pixel_dot(modes_re, modes_re) + pixel_dot(modes_im, modes_im)
    gram_im = pixel_dot(modes_re, modes_im) - pixel_dot(modes_im, modes_re)
    return (gram_re, gram_im)


def orthogonal_mix(gram_re, gram_im):
    mode_count = gram_re.shape[0]
    mode_power = jnp.diagonal(gram_re) + EPSILON
    inv_root = 1.0 / jnp.sqrt(mode_power)
    scale_mat = inv_root[:, None] * inv_root[None, :]
    norm_re = gram_re * scale_mat
    norm_im = gram_im * scale_mat
    embedded = jnp.concatenate(
        [jnp.concatenate([norm_re, -norm_im], axis=1), jnp.concatenate([norm_im, norm_re], axis=1)],
        axis=0,
    )
    frobenius = jnp.sqrt(jnp.sum(embedded * embedded))
    identity_mat = jnp.eye(2 * mode_count, dtype=jnp.float32)
    iterate_y = embedded / frobenius
    iterate_z = identity_mat
    def sweep(sweep_index, iterates):
        iterate_y, iterate_z = iterates
        correction = 1.5 * identity_mat - 0.5 * highest_dot(iterate_z, iterate_y)
        return (highest_dot(iterate_y, correction), highest_dot(correction, iterate_z))

    iterate_y, iterate_z = lax.fori_loop(0, NS_ITERS, sweep, (iterate_y, iterate_z))
    root_inv = iterate_z / jnp.sqrt(frobenius)
    weight_re = root_inv[:mode_count, :mode_count]
    weight_im = root_inv[mode_count:, :mode_count]
    ratio_mat = inv_root[:, None] * jnp.sqrt(mode_power)[None, :]
    return (weight_re * ratio_mat, weight_im * ratio_mat)


def onehot_place(starts, out_len, in_len):
    out_index = jnp.arange(out_len, dtype=jnp.int32)[None, :, None]
    in_index = jnp.arange(in_len, dtype=jnp.int32)[None, None, :]
    return (out_index == starts[:, None, None] + in_index).astype(jnp.bfloat16)


def split_parts(values):
    high = values.astype(jnp.bfloat16)
    rest = values - high.astype(jnp.float32)
    middle = rest.astype(jnp.bfloat16)
    low = (rest - middle.astype(jnp.float32)).astype(jnp.bfloat16)
    return jnp.stack([high, middle, low])


def exchange_sum(values, axis_name):
    count = lax.axis_size(axis_name)
    pieces = values.reshape(count, -1)
    mine = lax.all_to_all(pieces, axis_name, 0, 0, tiled=False).sum(axis=0)
    spread = jnp.broadcast_to(mine[None], pieces.shape)
    return lax.all_to_all(spread, axis_name, 0, 0, tiled=False).reshape(values.shape)


def shards(object_field, probe_modes, scan_offsets, measured):
    mode_index = lax.axis_index("mode")
    cos_t, sin_t = dft_tables(M)
    probe_re = probe_modes[0, 0]
    probe_im = probe_modes[1, 0]
    row_starts = scan_offsets[0]
    col_starts = scan_offsets[1]
    local_count = row_starts.shape[0]

    col_place = onehot_place(col_starts, object_field.shape[2], M)
    row_place = onehot_place(row_starts, object_field.shape[1], M)
    field_parts = split_parts(object_field)
    picked_cols = jnp.einsum(
        "pcik,jkb->pcijb", field_parts, col_place, preferred_element_type=jnp.float32
    ).astype(jnp.bfloat16)
    obj_patches = jnp.einsum(
        "jia,pcijb->pcjab", row_place, picked_cols, preferred_element_type=jnp.float32
    ).sum(axis=0)
    obj_re = obj_patches[0]
    obj_im = obj_patches[1]
    obj_norm = jnp.sum(obj_re * obj_re + obj_im * obj_im, axis=0)
    wave_re = (probe_re * obj_re - probe_im * obj_im).astype(jnp.bfloat16)
    wave_im = (probe_re * obj_im + probe_im * obj_re).astype(jnp.bfloat16)
    own_light = (probe_re * probe_re + probe_im * probe_im)[None]
    half_count = local_count // 2
    back_parts = []
    for half in range(2):
        chosen = slice(half * half_count, (half + 1) * half_count)
        far_re, far_im = forward_pass(wave_re[chosen], wave_im[chosen], cos_t, sin_t)
        mode_intensity = far_re * far_re + far_im * far_im
        if half == 0:
            summed = exchange_sum(jnp.concatenate([mode_intensity, own_light]), "mode")
            light_patch = summed[half_count:]
        else:
            summed = exchange_sum(mode_intensity, "mode")
        intensity = summed[:half_count]
        amp_ratio = jnp.sqrt(measured[chosen] / jnp.maximum(intensity, FLOOR_INTENSITY))
        factor = amp_ratio - 1.0
        spec_re = (factor * far_re).astype(jnp.bfloat16)
        spec_im = (factor * far_im).astype(jnp.bfloat16)
        back_parts.append(inverse_pass(spec_re, spec_im, cos_t, sin_t))
    back_re = jnp.concatenate([back_parts[0][0], back_parts[1][0]])
    back_im = jnp.concatenate([back_parts[0][1], back_parts[1][1]])
    grad_re = jnp.sum(obj_re * back_re + obj_im * back_im, axis=0)
    grad_im = jnp.sum(obj_re * back_im - obj_im * back_re, axis=0)
    patch_re = probe_re * back_re + probe_im * back_im
    patch_im = probe_re * back_im - probe_im * back_re

    rows_share = object_field.shape[1] // lax.axis_size("mode")
    patch_parts = split_parts(jnp.stack([patch_re, patch_im]))
    placed_rows = jnp.einsum(
        "jia,pcjab->pcjib", row_place, patch_parts, preferred_element_type=jnp.float32
    ).astype(jnp.bfloat16)
    grad_tile = jnp.einsum(
        "pcjib,jkb->pcik", placed_rows, col_place, preferred_element_type=jnp.float32
    ).sum(axis=0)
    own_place = onehot_place(row_starts - mode_index * rows_share, rows_share, M)
    light_parts = split_parts(light_patch[0])
    light_rows = jnp.einsum(
        "jia,pab->pjib", own_place, light_parts, preferred_element_type=jnp.float32
    ).astype(jnp.bfloat16)
    light_rows = jnp.einsum(
        "pjib,jkb->pik", light_rows, col_place, preferred_element_type=jnp.float32
    ).sum(axis=0)[None]
    own_rows = lax.dynamic_slice_in_dim(object_field, mode_index * rows_share, rows_share, 1)
    scan_count = lax.axis_size("scan")
    scan_index = lax.axis_index("scan")
    chunk_rows = M // scan_count
    grad_sums = jnp.stack([grad_re, grad_im, obj_norm]).reshape(3, scan_count, chunk_rows, M)
    grad_sums, grad_tile = lax.optimization_barrier((grad_sums, grad_tile))
    mode_count = lax.axis_size("mode")
    grad_sums = lax.all_to_all(grad_sums, "scan", 1, 1, tiled=False).sum(axis=1)
    probe_rows = lax.dynamic_slice_in_dim(probe_modes[:, 0], scan_index * chunk_rows, chunk_rows, 1)
    step_rows = probe_rows + grad_sums[0:2] / (grad_sums[2] + EPSILON)
    grad_blocks = grad_tile.reshape(2, mode_count, -1)
    block_size = grad_blocks.shape[2]
    spread_rows = jnp.broadcast_to(step_rows.reshape(2, 1, -1), (2, mode_count, chunk_rows * M))
    received = lax.all_to_all(
        jnp.concatenate([grad_blocks, spread_rows], axis=2), "mode", 1, 1, tiled=False
    )
    grad_rows = received[:, :, :block_size].sum(axis=1).reshape(2, rows_share, grad_tile.shape[2])
    object_new = own_rows + grad_rows / jnp.maximum(light_rows, FLOOR_ILLUM)
    every_rows = received[:, :, block_size:].reshape(2, mode_count, chunk_rows, M)
    rows_re = every_rows[0]
    rows_im = every_rows[1]
    gram_re, gram_im = gram_of(rows_re, rows_im)
    gram_pair = jnp.stack([gram_re, gram_im])
    spread_gram = jnp.broadcast_to(gram_pair[None], (scan_count,) + gram_pair.shape)
    gram_both = lax.all_to_all(spread_gram, "scan", 0, 0, tiled=False).sum(axis=0)
    mix_re, mix_im = orthogonal_mix(gram_both[0], gram_both[1])
    new_re = mix_all(mix_re, rows_re) - mix_all(mix_im, rows_im)
    new_im = mix_all(mix_re, rows_im) + mix_all(mix_im, rows_re)
    mine_rows = jnp.stack([
        lax.dynamic_index_in_dim(new_re, mode_index, 0, keepdims=False),
        lax.dynamic_index_in_dim(new_im, mode_index, 0, keepdims=False),
    ])
    spread_mine = jnp.broadcast_to(mine_rows[None], (scan_count,) + mine_rows.shape)
    all_rows = lax.all_to_all(spread_mine, "scan", 0, 0, tiled=False)
    probe_new = all_rows.transpose(1, 0, 2, 3).reshape(2, 1, M, M)
    return (object_new, probe_new)


def solution(mesh):
    placed = (
        P(None, "scan", None),
        P(None, "mode", None, None),
        P(None, "scan"),
        P("scan", None, None),
    )
    return jax.shard_map(
        shards,
        mesh=mesh,
        in_specs=placed,
        out_specs=(P(None, ("scan", "mode"), None), P(None, "mode", None, None)),
        check_vma=False,
    )
```

```python
import math

import jax
import jax.numpy as jnp
from jax import lax
from jax.sharding import PartitionSpec as P

M = 128
NS_ITERS = 8


FLOOR_INTENSITY = 0.1
FLOOR_ILLUM = 1.0
EPSILON = 1e-06


def dft_tables(length):
    pixel_index = jnp.arange(length, dtype=jnp.int32)
    product = pixel_index[:, None] * pixel_index[None, :] % length
    phase_angle = product.astype(jnp.float32) * (2.0 * math.pi / length)
    norm_scale = 1.0 / math.sqrt(length)
    return (
        (jnp.cos(phase_angle) * norm_scale).astype(jnp.bfloat16),
        (-jnp.sin(phase_angle) * norm_scale).astype(jnp.bfloat16),
    )


def right_product(left, table):
    return jnp.einsum("nab,bc->nac", left, table, preferred_element_type=jnp.float32)


def left_product(table, right):
    return jnp.einsum("ab,nbc->nac", table, right, preferred_element_type=jnp.float32)


def forward_pass(wave_re, wave_im, cos_t, sin_t):
    mid_re = (right_product(wave_re, cos_t) - right_product(wave_im, sin_t)).astype(jnp.bfloat16)
    mid_im = (right_product(wave_re, sin_t) + right_product(wave_im, cos_t)).astype(jnp.bfloat16)
    far_re = left_product(cos_t, mid_re) - left_product(sin_t, mid_im)
    far_im = left_product(sin_t, mid_re) + left_product(cos_t, mid_im)
    return (far_re, far_im)


def inverse_pass(spec_re, spec_im, cos_t, sin_t):
    half_re = (right_product(spec_re, cos_t) + right_product(spec_im, sin_t)).astype(jnp.bfloat16)
    half_im = (right_product(spec_im, cos_t) - right_product(spec_re, sin_t)).astype(jnp.bfloat16)
    back_re = left_product(cos_t, half_re) + left_product(sin_t, half_im)
    back_im = left_product(cos_t, half_im) - left_product(sin_t, half_re)
    return (back_re, back_im)


def highest_dot(left, right):
    return jnp.dot(left, right, precision=lax.Precision.HIGHEST, preferred_element_type=jnp.float32)


def pixel_dot(left, right):
    return jnp.einsum(
        "kab,lab->kl", left, right,
        precision=lax.Precision.HIGHEST, preferred_element_type=jnp.float32,
    )


def mix_all(weights, modes):
    return jnp.einsum(
        "lk,lab->kab", weights, modes,
        precision=lax.Precision.HIGHEST, preferred_element_type=jnp.float32,
    )


def gram_of(modes_re, modes_im):
    gram_re = pixel_dot(modes_re, modes_re) + pixel_dot(modes_im, modes_im)
    gram_im = pixel_dot(modes_re, modes_im) - pixel_dot(modes_im, modes_re)
    return (gram_re, gram_im)


def orthogonal_mix(gram_re, gram_im):
    mode_count = gram_re.shape[0]
    mode_power = jnp.diagonal(gram_re) + EPSILON
    inv_root = 1.0 / jnp.sqrt(mode_power)
    scale_mat = inv_root[:, None] * inv_root[None, :]
    norm_re = gram_re * scale_mat
    norm_im = gram_im * scale_mat
    embedded = jnp.concatenate(
        [jnp.concatenate([norm_re, -norm_im], axis=1), jnp.concatenate([norm_im, norm_re], axis=1)],
        axis=0,
    )
    frobenius = jnp.sqrt(jnp.sum(embedded * embedded))
    identity_mat = jnp.eye(2 * mode_count, dtype=jnp.float32)
    iterate_y = embedded / frobenius
    iterate_z = identity_mat
    def sweep(sweep_index, iterates):
        iterate_y, iterate_z = iterates
        correction = 1.5 * identity_mat - 0.5 * highest_dot(iterate_z, iterate_y)
        return (highest_dot(iterate_y, correction), highest_dot(correction, iterate_z))

    iterate_y, iterate_z = lax.fori_loop(0, NS_ITERS, sweep, (iterate_y, iterate_z))
    root_inv = iterate_z / jnp.sqrt(frobenius)
    weight_re = root_inv[:mode_count, :mode_count]
    weight_im = root_inv[mode_count:, :mode_count]
    ratio_mat = inv_root[:, None] * jnp.sqrt(mode_power)[None, :]
    return (weight_re * ratio_mat, weight_im * ratio_mat)


def onehot_place(starts, out_len, in_len):
    out_index = jnp.arange(out_len, dtype=jnp.int32)[None, :, None]
    in_index = jnp.arange(in_len, dtype=jnp.int32)[None, None, :]
    return (out_index == starts[:, None, None] + in_index).astype(jnp.bfloat16)


def split_parts(values):
    high = values.astype(jnp.bfloat16)
    rest = values - high.astype(jnp.float32)
    middle = rest.astype(jnp.bfloat16)
    low = (rest - middle.astype(jnp.float32)).astype(jnp.bfloat16)
    return jnp.stack([high, middle, low])


def exchange_sum(values, axis_name):
    count = lax.axis_size(axis_name)
    pieces = values.reshape(count, -1)
    mine = lax.all_to_all(pieces, axis_name, 0, 0, tiled=False).sum(axis=0)
    spread = jnp.broadcast_to(mine[None], pieces.shape)
    return lax.all_to_all(spread, axis_name, 0, 0, tiled=False).reshape(values.shape)


def shards(object_field, probe_modes, scan_offsets, measured):
    mode_index = lax.axis_index("mode")
    cos_t, sin_t = dft_tables(M)
    probe_re = probe_modes[0, 0]
    probe_im = probe_modes[1, 0]
    row_starts = scan_offsets[0]
    col_starts = scan_offsets[1]
    local_count = row_starts.shape[0]

    col_place = onehot_place(col_starts, object_field.shape[2], M)
    row_place = onehot_place(row_starts, object_field.shape[1], M)
    field_parts = split_parts(object_field)
    picked_cols = jnp.einsum(
        "pcik,jkb->pcijb", field_parts, col_place, preferred_element_type=jnp.float32
    ).astype(jnp.bfloat16)
    obj_patches = jnp.einsum(
        "jia,pcijb->pcjab", row_place, picked_cols, preferred_element_type=jnp.float32
    ).sum(axis=0)
    obj_re = obj_patches[0]
    obj_im = obj_patches[1]
    obj_norm = jnp.sum(obj_re * obj_re + obj_im * obj_im, axis=0)
    wave_re = (probe_re * obj_re - probe_im * obj_im).astype(jnp.bfloat16)
    wave_im = (probe_re * obj_im + probe_im * obj_re).astype(jnp.bfloat16)
    far_re, far_im = forward_pass(wave_re, wave_im, cos_t, sin_t)
    mode_intensity = far_re * far_re + far_im * far_im
    own_light = (probe_re * probe_re + probe_im * probe_im)[None]
    summed = exchange_sum(jnp.concatenate([mode_intensity, own_light]), "mode")
    intensity = summed[:local_count]
    light_patch = summed[local_count:]
    amp_ratio = jnp.sqrt(measured / jnp.maximum(intensity, FLOOR_INTENSITY))
    factor = amp_ratio - 1.0
    spec_re = (factor * far_re).astype(jnp.bfloat16)
    spec_im = (factor * far_im).astype(jnp.bfloat16)
    back_re, back_im = inverse_pass(spec_re, spec_im, cos_t, sin_t)
    grad_re = jnp.sum(obj_re * back_re + obj_im * back_im, axis=0)
    grad_im = jnp.sum(obj_re * back_im - obj_im * back_re, axis=0)
    patch_re = probe_re * back_re + probe_im * back_im
    patch_im = probe_re * back_im - probe_im * back_re

    rows_share = object_field.shape[1] // lax.axis_size("mode")
    patch_parts = split_parts(jnp.stack([patch_re, patch_im]))
    placed_rows = jnp.einsum(
        "jia,pcjab->pcjib", row_place, patch_parts, preferred_element_type=jnp.float32
    ).astype(jnp.bfloat16)
    grad_tile = jnp.einsum(
        "pcjib,jkb->pcik", placed_rows, col_place, preferred_element_type=jnp.float32
    ).sum(axis=0)
    own_place = onehot_place(row_starts - mode_index * rows_share, rows_share, M)
    light_parts = split_parts(light_patch[0])
    light_rows = jnp.einsum(
        "jia,pab->pjib", own_place, light_parts, preferred_element_type=jnp.float32
    ).astype(jnp.bfloat16)
    light_rows = jnp.einsum(
        "pjib,jkb->pik", light_rows, col_place, preferred_element_type=jnp.float32
    ).sum(axis=0)[None]
    own_rows = lax.dynamic_slice_in_dim(object_field, mode_index * rows_share, rows_share, 1)
    scan_count = lax.axis_size("scan")
    scan_index = lax.axis_index("scan")
    chunk_rows = M // scan_count
    grad_sums = jnp.stack([grad_re, grad_im, obj_norm]).reshape(3, scan_count, chunk_rows, M)
    grad_sums, grad_tile = lax.optimization_barrier((grad_sums, grad_tile))
    mode_count = lax.axis_size("mode")
    grad_sums = lax.all_to_all(grad_sums, "scan", 1, 1, tiled=False).sum(axis=1)
    probe_rows = lax.dynamic_slice_in_dim(probe_modes[:, 0], scan_index * chunk_rows, chunk_rows, 1)
    step_rows = probe_rows + grad_sums[0:2] / (grad_sums[2] + EPSILON)
    grad_blocks = grad_tile.reshape(2, mode_count, -1)
    block_size = grad_blocks.shape[2]
    spread_rows = jnp.broadcast_to(step_rows.reshape(2, 1, -1), (2, mode_count, chunk_rows * M))
    received = lax.all_to_all(
        jnp.concatenate([grad_blocks, spread_rows], axis=2), "mode", 1, 1, tiled=False
    )
    grad_rows = received[:, :, :block_size].sum(axis=1).reshape(2, rows_share, grad_tile.shape[2])
    object_new = own_rows + grad_rows / jnp.maximum(light_rows, FLOOR_ILLUM)
    every_rows = received[:, :, block_size:].reshape(2, mode_count, chunk_rows, M)
    rows_re = every_rows[0]
    rows_im = every_rows[1]
    gram_re, gram_im = gram_of(rows_re, rows_im)
    gram_pair = jnp.stack([gram_re, gram_im])
    spread_gram = jnp.broadcast_to(gram_pair[None], (scan_count,) + gram_pair.shape)
    gram_both = lax.all_to_all(spread_gram, "scan", 0, 0, tiled=False).sum(axis=0)
    mix_re, mix_im = orthogonal_mix(gram_both[0], gram_both[1])
    new_re = mix_all(mix_re, rows_re) - mix_all(mix_im, rows_im)
    new_im = mix_all(mix_re, rows_im) + mix_all(mix_im, rows_re)
    mine_rows = jnp.stack([
        lax.dynamic_index_in_dim(new_re, mode_index, 0, keepdims=False),
        lax.dynamic_index_in_dim(new_im, mode_index, 0, keepdims=False),
    ])
    spread_mine = jnp.broadcast_to(mine_rows[None], (scan_count,) + mine_rows.shape)
    all_rows = lax.all_to_all(spread_mine, "scan", 0, 0, tiled=False)
    probe_new = all_rows.transpose(1, 0, 2, 3).reshape(2, 1, M, M)
    return (object_new, probe_new)


def solution(mesh):
    placed = (
        P(None, "scan", None),
        P(None, "mode", None, None),
        P(None, "scan"),
        P("scan", None, None),
    )
    return jax.shard_map(
        shards,
        mesh=mesh,
        in_specs=placed,
        out_specs=(P(None, ("scan", "mode"), None), P(None, "mode", None, None)),
        check_vma=False,
    )
```

```python
import math

import jax
import jax.numpy as jnp
from jax import lax
from jax.sharding import PartitionSpec as P

M = 128
NS_ITERS = 8


FLOOR_INTENSITY = 0.1
FLOOR_ILLUM = 1.0
EPSILON = 1e-06


def dft_tables(length):
    pixel_index = jnp.arange(length, dtype=jnp.int32)
    product = pixel_index[:, None] * pixel_index[None, :] % length
    phase_angle = product.astype(jnp.float32) * (2.0 * math.pi / length)
    norm_scale = 1.0 / math.sqrt(length)
    return (
        (jnp.cos(phase_angle) * norm_scale).astype(jnp.bfloat16),
        (-jnp.sin(phase_angle) * norm_scale).astype(jnp.bfloat16),
    )


def right_product(left, table):
    return jnp.einsum("nab,bc->nac", left, table, preferred_element_type=jnp.float32)


def left_product(table, right):
    return jnp.einsum("ab,nbc->nac", table, right, preferred_element_type=jnp.float32)


def forward_pass(wave_re, wave_im, cos_t, sin_t):
    mid_re = (right_product(wave_re, cos_t) - right_product(wave_im, sin_t)).astype(jnp.bfloat16)
    mid_im = (right_product(wave_re, sin_t) + right_product(wave_im, cos_t)).astype(jnp.bfloat16)
    far_re = left_product(cos_t, mid_re) - left_product(sin_t, mid_im)
    far_im = left_product(sin_t, mid_re) + left_product(cos_t, mid_im)
    return (far_re, far_im)


def inverse_pass(spec_re, spec_im, cos_t, sin_t):
    half_re = (right_product(spec_re, cos_t) + right_product(spec_im, sin_t)).astype(jnp.bfloat16)
    half_im = (right_product(spec_im, cos_t) - right_product(spec_re, sin_t)).astype(jnp.bfloat16)
    back_re = left_product(cos_t, half_re) + left_product(sin_t, half_im)
    back_im = left_product(cos_t, half_im) - left_product(sin_t, half_re)
    return (back_re, back_im)


def highest_dot(left, right):
    return jnp.dot(left, right, precision=lax.Precision.HIGHEST, preferred_element_type=jnp.float32)


def pixel_dot(left, right):
    return jnp.einsum(
        "kab,lab->kl", left, right,
        precision=lax.Precision.HIGHEST, preferred_element_type=jnp.float32,
    )


def mix_all(weights, modes):
    return jnp.einsum(
        "lk,lab->kab", weights, modes,
        precision=lax.Precision.HIGHEST, preferred_element_type=jnp.float32,
    )


def gram_of(modes_re, modes_im):
    gram_re = pixel_dot(modes_re, modes_re) + pixel_dot(modes_im, modes_im)
    gram_im = pixel_dot(modes_re, modes_im) - pixel_dot(modes_im, modes_re)
    return (gram_re, gram_im)


def orthogonal_mix(gram_re, gram_im):
    mode_count = gram_re.shape[0]
    mode_power = jnp.diagonal(gram_re) + EPSILON
    inv_root = 1.0 / jnp.sqrt(mode_power)
    scale_mat = inv_root[:, None] * inv_root[None, :]
    norm_re = gram_re * scale_mat
    norm_im = gram_im * scale_mat
    embedded = jnp.concatenate(
        [jnp.concatenate([norm_re, -norm_im], axis=1), jnp.concatenate([norm_im, norm_re], axis=1)],
        axis=0,
    )
    frobenius = jnp.sqrt(jnp.sum(embedded * embedded))
    identity_mat = jnp.eye(2 * mode_count, dtype=jnp.float32)
    iterate_y = embedded / frobenius
    iterate_z = identity_mat
    def sweep(sweep_index, iterates):
        iterate_y, iterate_z = iterates
        correction = 1.5 * identity_mat - 0.5 * highest_dot(iterate_z, iterate_y)
        return (highest_dot(iterate_y, correction), highest_dot(correction, iterate_z))

    iterate_y, iterate_z = lax.fori_loop(0, NS_ITERS, sweep, (iterate_y, iterate_z))
    root_inv = iterate_z / jnp.sqrt(frobenius)
    weight_re = root_inv[:mode_count, :mode_count]
    weight_im = root_inv[mode_count:, :mode_count]
    ratio_mat = inv_root[:, None] * jnp.sqrt(mode_power)[None, :]
    return (weight_re * ratio_mat, weight_im * ratio_mat)


def onehot_place(starts, out_len, in_len):
    out_index = jnp.arange(out_len, dtype=jnp.int32)[None, :, None]
    in_index = jnp.arange(in_len, dtype=jnp.int32)[None, None, :]
    return (out_index == starts[:, None, None] + in_index).astype(jnp.bfloat16)


def split_parts(values):
    high = values.astype(jnp.bfloat16)
    rest = values - high.astype(jnp.float32)
    middle = rest.astype(jnp.bfloat16)
    low = (rest - middle.astype(jnp.float32)).astype(jnp.bfloat16)
    return jnp.stack([high, middle, low])


def exchange_sum(values, axis_name):
    count = lax.axis_size(axis_name)
    pieces = values.reshape(count, -1)
    mine = lax.all_to_all(pieces, axis_name, 0, 0, tiled=False).sum(axis=0)
    spread = jnp.broadcast_to(mine[None], pieces.shape)
    return lax.all_to_all(spread, axis_name, 0, 0, tiled=False).reshape(values.shape)


def shards(object_field, probe_modes, scan_offsets, measured):
    mode_index = lax.axis_index("mode")
    cos_t, sin_t = dft_tables(M)
    probe_re = probe_modes[0, 0]
    probe_im = probe_modes[1, 0]
    row_starts = scan_offsets[0]
    col_starts = scan_offsets[1]
    local_count = row_starts.shape[0]

    col_place = onehot_place(col_starts, object_field.shape[2], M)
    row_place = onehot_place(row_starts, object_field.shape[1], M)
    field_parts = split_parts(object_field)
    picked_cols = jnp.einsum(
        "pcik,jkb->pcijb", field_parts, col_place, preferred_element_type=jnp.float32
    ).astype(jnp.bfloat16)
    obj_patches = jnp.einsum(
        "jia,pcijb->pcjab", row_place, picked_cols, preferred_element_type=jnp.float32
    ).sum(axis=0)
    obj_re = obj_patches[0]
    obj_im = obj_patches[1]
    obj_norm = jnp.sum(obj_re * obj_re + obj_im * obj_im, axis=0)
    wave_re = (probe_re * obj_re - probe_im * obj_im).astype(jnp.bfloat16)
    wave_im = (probe_re * obj_im + probe_im * obj_re).astype(jnp.bfloat16)
    far_re, far_im = forward_pass(wave_re, wave_im, cos_t, sin_t)
    mode_intensity = far_re * far_re + far_im * far_im
    own_light = (probe_re * probe_re + probe_im * probe_im)[None]
    summed = exchange_sum(jnp.concatenate([mode_intensity, own_light]), "mode")
    intensity = summed[:local_count]
    light_patch = summed[local_count:]
    amp_ratio = jnp.sqrt(measured / jnp.maximum(intensity, FLOOR_INTENSITY))
    factor = amp_ratio - 1.0
    spec_re = (factor * far_re).astype(jnp.bfloat16)
    spec_im = (factor * far_im).astype(jnp.bfloat16)
    back_re, back_im = inverse_pass(spec_re, spec_im, cos_t, sin_t)
    grad_re = jnp.sum(obj_re * back_re + obj_im * back_im, axis=0)
    grad_im = jnp.sum(obj_re * back_im - obj_im * back_re, axis=0)
    patch_re = probe_re * back_re + probe_im * back_im
    patch_im = probe_re * back_im - probe_im * back_re

    rows_share = object_field.shape[1] // lax.axis_size("mode")
    patch_parts = split_parts(jnp.stack([patch_re, patch_im]))
    placed_rows = jnp.einsum(
        "jia,pcjab->pcjib", row_place, patch_parts, preferred_element_type=jnp.float32
    ).astype(jnp.bfloat16)
    grad_tile = jnp.einsum(
        "pcjib,jkb->pcik", placed_rows, col_place, preferred_element_type=jnp.float32
    ).sum(axis=0)
    own_place = onehot_place(row_starts - mode_index * rows_share, rows_share, M)
    light_parts = split_parts(light_patch[0])
    light_rows = jnp.einsum(
        "jia,pab->pjib", own_place, light_parts, preferred_element_type=jnp.float32
    ).astype(jnp.bfloat16)
    light_rows = jnp.einsum(
        "pjib,jkb->pik", light_rows, col_place, preferred_element_type=jnp.float32
    ).sum(axis=0)[None]
    own_rows = lax.dynamic_slice_in_dim(object_field, mode_index * rows_share, rows_share, 1)
    scan_count = lax.axis_size("scan")
    scan_index = lax.axis_index("scan")
    chunk_rows = M // scan_count
    grad_sums = jnp.stack([grad_re, grad_im, obj_norm]).reshape(3, scan_count, chunk_rows, M)
    mode_count = lax.axis_size("mode")
    grad_sums = lax.all_to_all(grad_sums, "scan", 1, 1, tiled=False).sum(axis=1)
    probe_rows = lax.dynamic_slice_in_dim(probe_modes[:, 0], scan_index * chunk_rows, chunk_rows, 1)
    step_rows = probe_rows + grad_sums[0:2] / (grad_sums[2] + EPSILON)
    grad_blocks = grad_tile.reshape(2, mode_count, -1)
    block_size = grad_blocks.shape[2]
    spread_rows = jnp.broadcast_to(step_rows.reshape(2, 1, -1), (2, mode_count, chunk_rows * M))
    received = lax.all_to_all(
        jnp.concatenate([grad_blocks, spread_rows], axis=2), "mode", 1, 1, tiled=False
    )
    grad_rows = received[:, :, :block_size].sum(axis=1).reshape(2, rows_share, grad_tile.shape[2])
    object_new = own_rows + grad_rows / jnp.maximum(light_rows, FLOOR_ILLUM)
    every_rows = received[:, :, block_size:].reshape(2, mode_count, chunk_rows, M)
    rows_re = every_rows[0]
    rows_im = every_rows[1]
    gram_re, gram_im = gram_of(rows_re, rows_im)
    gram_pair = jnp.stack([gram_re, gram_im])
    spread_gram = jnp.broadcast_to(gram_pair[None], (scan_count,) + gram_pair.shape)
    gram_both = lax.all_to_all(spread_gram, "scan", 0, 0, tiled=False).sum(axis=0)
    mix_re, mix_im = orthogonal_mix(gram_both[0], gram_both[1])
    new_re = mix_all(mix_re, rows_re) - mix_all(mix_im, rows_im)
    new_im = mix_all(mix_re, rows_im) + mix_all(mix_im, rows_re)
    mine_rows = jnp.stack([
        lax.dynamic_index_in_dim(new_re, mode_index, 0, keepdims=False),
        lax.dynamic_index_in_dim(new_im, mode_index, 0, keepdims=False),
    ])
    spread_mine = jnp.broadcast_to(mine_rows[None], (scan_count,) + mine_rows.shape)
    all_rows = lax.all_to_all(spread_mine, "scan", 0, 0, tiled=False)
    probe_new = all_rows.transpose(1, 0, 2, 3).reshape(2, 1, M, M)
    return (object_new, probe_new)


def solution(mesh):
    placed = (
        P(None, "scan", None),
        P(None, "mode", None, None),
        P(None, "scan"),
        P("scan", None, None),
    )
    return jax.shard_map(
        shards,
        mesh=mesh,
        in_specs=placed,
        out_specs=(P(None, ("scan", "mode"), None), P(None, "mode", None, None)),
        check_vma=False,
    )
```

```python
import math

import jax
import jax.numpy as jnp
from jax import lax
from jax.sharding import PartitionSpec as P

M = 128
NS_ITERS = 8


FLOOR_INTENSITY = 0.1
FLOOR_ILLUM = 1.0
EPSILON = 1e-06


def dft_tables(length):
    pixel_index = jnp.arange(length, dtype=jnp.int32)
    product = pixel_index[:, None] * pixel_index[None, :] % length
    phase_angle = product.astype(jnp.float32) * (2.0 * math.pi / length)
    norm_scale = 1.0 / math.sqrt(length)
    return (
        (jnp.cos(phase_angle) * norm_scale).astype(jnp.bfloat16),
        (-jnp.sin(phase_angle) * norm_scale).astype(jnp.bfloat16),
    )


def right_product(left, table):
    return jnp.einsum("nab,bc->nac", left, table, preferred_element_type=jnp.float32)


def left_product(table, right):
    return jnp.einsum("ab,nbc->nac", table, right, preferred_element_type=jnp.float32)


def forward_pass(wave_re, wave_im, cos_t, sin_t):
    mid_re = (right_product(wave_re, cos_t) - right_product(wave_im, sin_t)).astype(jnp.bfloat16)
    mid_im = (right_product(wave_re, sin_t) + right_product(wave_im, cos_t)).astype(jnp.bfloat16)
    far_re = left_product(cos_t, mid_re) - left_product(sin_t, mid_im)
    far_im = left_product(sin_t, mid_re) + left_product(cos_t, mid_im)
    return (far_re, far_im)


def inverse_pass(spec_re, spec_im, cos_t, sin_t):
    half_re = (right_product(spec_re, cos_t) + right_product(spec_im, sin_t)).astype(jnp.bfloat16)
    half_im = (right_product(spec_im, cos_t) - right_product(spec_re, sin_t)).astype(jnp.bfloat16)
    back_re = left_product(cos_t, half_re) + left_product(sin_t, half_im)
    back_im = left_product(cos_t, half_im) - left_product(sin_t, half_re)
    return (back_re, back_im)


def highest_dot(left, right):
    return jnp.dot(left, right, precision=lax.Precision.HIGH, preferred_element_type=jnp.float32)


def pixel_dot(left, right):
    return jnp.einsum(
        "kab,lab->kl", left, right,
        precision=lax.Precision.HIGH, preferred_element_type=jnp.float32,
    )


def mix_all(weights, modes):
    return jnp.einsum(
        "lk,lab->kab", weights, modes,
        precision=lax.Precision.HIGH, preferred_element_type=jnp.float32,
    )


def gram_of(modes_re, modes_im):
    gram_re = pixel_dot(modes_re, modes_re) + pixel_dot(modes_im, modes_im)
    gram_im = pixel_dot(modes_re, modes_im) - pixel_dot(modes_im, modes_re)
    return (gram_re, gram_im)


def orthogonal_mix(gram_re, gram_im):
    mode_count = gram_re.shape[0]
    mode_power = jnp.diagonal(gram_re) + EPSILON
    inv_root = 1.0 / jnp.sqrt(mode_power)
    scale_mat = inv_root[:, None] * inv_root[None, :]
    norm_re = gram_re * scale_mat
    norm_im = gram_im * scale_mat
    embedded = jnp.concatenate(
        [jnp.concatenate([norm_re, -norm_im], axis=1), jnp.concatenate([norm_im, norm_re], axis=1)],
        axis=0,
    )
    frobenius = jnp.sqrt(jnp.sum(embedded * embedded))
    identity_mat = jnp.eye(2 * mode_count, dtype=jnp.float32)
    iterate_y = embedded / frobenius
    iterate_z = identity_mat
    def sweep(sweep_index, iterates):
        iterate_y, iterate_z = iterates
        correction = 1.5 * identity_mat - 0.5 * highest_dot(iterate_z, iterate_y)
        return (highest_dot(iterate_y, correction), highest_dot(correction, iterate_z))

    iterate_y, iterate_z = lax.fori_loop(0, NS_ITERS, sweep, (iterate_y, iterate_z))
    root_inv = iterate_z / jnp.sqrt(frobenius)
    weight_re = root_inv[:mode_count, :mode_count]
    weight_im = root_inv[mode_count:, :mode_count]
    ratio_mat = inv_root[:, None] * jnp.sqrt(mode_power)[None, :]
    return (weight_re * ratio_mat, weight_im * ratio_mat)


def onehot_place(starts, out_len, in_len):
    out_index = jnp.arange(out_len, dtype=jnp.int32)[None, :, None]
    in_index = jnp.arange(in_len, dtype=jnp.int32)[None, None, :]
    return (out_index == starts[:, None, None] + in_index).astype(jnp.bfloat16)


def split_parts(values):
    high = values.astype(jnp.bfloat16)
    rest = values - high.astype(jnp.float32)
    middle = rest.astype(jnp.bfloat16)
    low = (rest - middle.astype(jnp.float32)).astype(jnp.bfloat16)
    return jnp.stack([high, middle, low])


def exchange_sum(values, axis_name):
    count = lax.axis_size(axis_name)
    pieces = values.reshape(count, -1)
    mine = lax.all_to_all(pieces, axis_name, 0, 0, tiled=False).sum(axis=0)
    spread = jnp.broadcast_to(mine[None], pieces.shape)
    return lax.all_to_all(spread, axis_name, 0, 0, tiled=False).reshape(values.shape)


def shards(object_field, probe_modes, scan_offsets, measured):
    mode_index = lax.axis_index("mode")
    cos_t, sin_t = dft_tables(M)
    probe_re = probe_modes[0, 0]
    probe_im = probe_modes[1, 0]
    row_starts = scan_offsets[0]
    col_starts = scan_offsets[1]
    local_count = row_starts.shape[0]

    col_place = onehot_place(col_starts, object_field.shape[2], M)
    row_place = onehot_place(row_starts, object_field.shape[1], M)
    field_parts = split_parts(object_field)
    picked_cols = jnp.einsum(
        "pcik,jkb->pcijb", field_parts, col_place, preferred_element_type=jnp.float32
    ).astype(jnp.bfloat16)
    obj_patches = jnp.einsum(
        "jia,pcijb->pcjab", row_place, picked_cols, preferred_element_type=jnp.float32
    ).sum(axis=0)
    obj_re = obj_patches[0]
    obj_im = obj_patches[1]
    obj_norm = jnp.sum(obj_re * obj_re + obj_im * obj_im, axis=0)
    wave_re = (probe_re * obj_re - probe_im * obj_im).astype(jnp.bfloat16)
    wave_im = (probe_re * obj_im + probe_im * obj_re).astype(jnp.bfloat16)
    far_re, far_im = forward_pass(wave_re, wave_im, cos_t, sin_t)
    mode_intensity = far_re * far_re + far_im * far_im
    own_light = (probe_re * probe_re + probe_im * probe_im)[None]
    summed = exchange_sum(jnp.concatenate([mode_intensity, own_light]), "mode")
    intensity = summed[:local_count]
    light_patch = summed[local_count:]
    amp_ratio = jnp.sqrt(measured / jnp.maximum(intensity, FLOOR_INTENSITY))
    factor = amp_ratio - 1.0
    spec_re = (factor * far_re).astype(jnp.bfloat16)
    spec_im = (factor * far_im).astype(jnp.bfloat16)
    back_re, back_im = inverse_pass(spec_re, spec_im, cos_t, sin_t)
    grad_re = jnp.sum(obj_re * back_re + obj_im * back_im, axis=0)
    grad_im = jnp.sum(obj_re * back_im - obj_im * back_re, axis=0)
    patch_re = probe_re * back_re + probe_im * back_im
    patch_im = probe_re * back_im - probe_im * back_re

    rows_share = object_field.shape[1] // lax.axis_size("mode")
    patch_parts = split_parts(jnp.stack([patch_re, patch_im]))
    placed_rows = jnp.einsum(
        "jia,pcjab->pcjib", row_place, patch_parts, preferred_element_type=jnp.float32
    ).astype(jnp.bfloat16)
    grad_tile = jnp.einsum(
        "pcjib,jkb->pcik", placed_rows, col_place, preferred_element_type=jnp.float32
    ).sum(axis=0)
    own_place = onehot_place(row_starts - mode_index * rows_share, rows_share, M)
    light_parts = split_parts(light_patch[0])
    light_rows = jnp.einsum(
        "jia,pab->pjib", own_place, light_parts, preferred_element_type=jnp.float32
    ).astype(jnp.bfloat16)
    light_rows = jnp.einsum(
        "pjib,jkb->pik", light_rows, col_place, preferred_element_type=jnp.float32
    ).sum(axis=0)[None]
    own_rows = lax.dynamic_slice_in_dim(object_field, mode_index * rows_share, rows_share, 1)
    scan_count = lax.axis_size("scan")
    scan_index = lax.axis_index("scan")
    chunk_rows = M // scan_count
    grad_sums = jnp.stack([grad_re, grad_im, obj_norm]).reshape(3, scan_count, chunk_rows, M)
    mode_count = lax.axis_size("mode")
    grad_sums = lax.all_to_all(grad_sums, "scan", 1, 1, tiled=False).sum(axis=1)
    probe_rows = lax.dynamic_slice_in_dim(probe_modes[:, 0], scan_index * chunk_rows, chunk_rows, 1)
    step_rows = probe_rows + grad_sums[0:2] / (grad_sums[2] + EPSILON)
    grad_blocks = grad_tile.reshape(2, mode_count, -1)
    block_size = grad_blocks.shape[2]
    spread_rows = jnp.broadcast_to(step_rows.reshape(2, 1, -1), (2, mode_count, chunk_rows * M))
    received = lax.all_to_all(
        jnp.concatenate([grad_blocks, spread_rows], axis=2), "mode", 1, 1, tiled=False
    )
    grad_rows = received[:, :, :block_size].sum(axis=1).reshape(2, rows_share, grad_tile.shape[2])
    object_new = own_rows + grad_rows / jnp.maximum(light_rows, FLOOR_ILLUM)
    every_rows = received[:, :, block_size:].reshape(2, mode_count, chunk_rows, M)
    rows_re = every_rows[0]
    rows_im = every_rows[1]
    gram_re, gram_im = gram_of(rows_re, rows_im)
    gram_pair = jnp.stack([gram_re, gram_im])
    spread_gram = jnp.broadcast_to(gram_pair[None], (scan_count,) + gram_pair.shape)
    gram_both = lax.all_to_all(spread_gram, "scan", 0, 0, tiled=False).sum(axis=0)
    mix_re, mix_im = orthogonal_mix(gram_both[0], gram_both[1])
    new_re = mix_all(mix_re, rows_re) - mix_all(mix_im, rows_im)
    new_im = mix_all(mix_re, rows_im) + mix_all(mix_im, rows_re)
    mine_rows = jnp.stack([
        lax.dynamic_index_in_dim(new_re, mode_index, 0, keepdims=False),
        lax.dynamic_index_in_dim(new_im, mode_index, 0, keepdims=False),
    ])
    spread_mine = jnp.broadcast_to(mine_rows[None], (scan_count,) + mine_rows.shape)
    all_rows = lax.all_to_all(spread_mine, "scan", 0, 0, tiled=False)
    probe_new = all_rows.transpose(1, 0, 2, 3).reshape(2, 1, M, M)
    return (object_new, probe_new)


def solution(mesh):
    placed = (
        P(None, "scan", None),
        P(None, "mode", None, None),
        P(None, "scan"),
        P("scan", None, None),
    )
    return jax.shard_map(
        shards,
        mesh=mesh,
        in_specs=placed,
        out_specs=(P(None, ("scan", "mode"), None), P(None, "mode", None, None)),
        check_vma=False,
    )
```
